512 devices in a mesh: seq: 128 (over y, z, core), head: 4 (over x).
Axes of the slice: x: 4, y: 8, z: 8, core: 2. Of those that a mesh axis runs over, the one named last changes fastest.
Arguments:
- query_tokens: bfloat16 [32768, 512], P('seq', 'head'), parts along dimension 1, may hold values from -27 to 27
- key_tokens: bfloat16 [32768, 512], P('seq', 'head'), parts along dimension 1, may hold values from -8 to 8
- value_tokens: bfloat16 [32768, 512], P('seq', 'head'), parts along dimension 1, may hold values from -6 to 6
- grad_out: bfloat16 [32768, 512], P('seq', 'head'), parts along dimension 1, may hold values from -6 to 6
- far_block: int32 [128, 128, 2], replicated, may hold values from -1 to 1, as said below
Outputs:
- attention_out: float32 [32768, 512], P('seq', 'head'), parts along dimension 1
- query_grad: float32 [32768, 512], P('seq', 'head'), parts along dimension 1
- key_grad: float32 [32768, 512], P('seq', 'head'), parts along dimension 1
- value_grad: float32 [32768, 512], P('seq', 'head'), parts along dimension 1
The draws below stay inside these ranges and needn't reach their ends.
There are 4 independent parts, one for each index of `head`. The reference program is written for one: setup_inputs(seed, part) draws one part's arguments, and reference() takes and returns one part's arrays. A program takes and returns all parts, laid end to end along the dimension named above; an argument that names none is the same for every part. Nothing has to cross between parts.
Inputs may be any that keep to these rules, and one draw needn't show every extreme that they name: `far_block`: entry (f, g, b) is -1 unless |f - g| is 2, 3 or a power of two from 4 up to below 128. For each (f, g) either both entries are -1, or entry b equals b (query block b of frame f sees block b of frame g).
All inputs are finite; a program needn't handle non-finite values.
Results may differ from the reference program's by a relative error of at most 0.012.
The reference program's roundings to bfloat16 on the way (of `weights` and `dscores`) count: a program that leaves them out, or rounds other values in their place, can miss the bound.
Values may be sent and summed in bfloat16 or wider, within the bound.
No kernel may reach another device: no remote copies, remote signals or barrier semaphores. Data moves between devices by JAX's collectives and lax.ppermute only.
A program may use at most 64 MiB of HBM per device.

```python
import jax
import jax.numpy as jnp
from jax import lax

HD = 128
TOK_DEV = 256
BLK = 128
FRAMES = 128
TOKENS = 32768


def draw_query_tokens(key, part):
    base_key = jax.random.fold_in(key, 1)
    return (1.6 * jnp.clip(jax.random.normal(base_key, (TOKENS, HD), jnp.float32), -5.0, 5.0)).astype(jnp.bfloat16)


def draw_key_tokens(key, part):
    base_key = jax.random.fold_in(key, 2)
    return (1.6 * jnp.clip(jax.random.normal(base_key, (TOKENS, HD), jnp.float32), -5.0, 5.0)).astype(jnp.bfloat16)


def draw_far_block(key, part):
    frame_count = FRAMES
    tile_count = TOK_DEV // BLK
    frame_ids = jnp.arange(frame_count, dtype=jnp.int32)
    distance = jnp.abs(frame_ids[:, None] - frame_ids[None, :])
    allowed = (distance == 2) | (distance == 3)
    power_step = 4
    while power_step < frame_count:
        allowed = allowed | (distance == power_step)
        power_step = power_step * 2
    window_first = jax.random.randint(jax.random.fold_in(key, 3), (frame_count, frame_count), 0, tile_count - 1, dtype=jnp.int32)
    window_first = window_first.at[0, 2].set(tile_count - 2)
    drop_draw = jax.random.randint(jax.random.fold_in(key, 4), (frame_count, frame_count), 0, 4, dtype=jnp.int32)
    kept = allowed & ((distance < 8) | (drop_draw > 0))
    tile_ids = jnp.arange(tile_count, dtype=jnp.int32)
    chosen = jnp.clip(tile_ids[None, None, :], window_first[:, :, None], window_first[:, :, None] + 1)
    return jnp.where(kept[:, :, None], chosen, -1).astype(jnp.int32)


def block_levels(stream_key, dims, shards, low, high):
    gain, own = 1.0, jax.random.fold_in(stream_key, 6)
    for position, parts in shards:
        steps = jnp.exp(jax.random.uniform(jax.random.fold_in(own, position), (parts,), jnp.float32, low / len(shards), high / len(shards)))
        gain = gain * jnp.repeat(steps, dims[position] // parts).reshape([-1 if axis == position else 1 for axis in range(len(dims))])
    return gain


def bell_draw(key, dims, width, most, cuts=(), held_as=jnp.bfloat16):
    level = block_levels(key, dims, cuts, -0.22, 0.18) if cuts else 1.0
    drawn = jax.random.normal(key, dims, jnp.float32) * width * level
    return jnp.minimum(jnp.maximum(drawn, -most), most).astype(held_as)


def setup_inputs(seed: int = 0, part: int = 0) -> dict:
    seeds = jax.random.split(jax.random.key(seed), 6)
    own_keys = jax.random.split(jax.random.fold_in(seeds[5], part), 6)
    query_tokens = draw_query_tokens(jax.random.fold_in(jax.random.fold_in(seeds[5], part), 71), part)
    key_tokens = draw_key_tokens(jax.random.fold_in(jax.random.fold_in(seeds[5], part), 71), part)
    value_tokens = bell_draw(own_keys[2], (TOKENS, HD), 1.0, 6.0, ((0, 128),))
    grad_out = bell_draw(own_keys[3], (TOKENS, HD), 1.0, 6.0, ((0, 128),))
    far_block = draw_far_block(jax.random.fold_in(seeds[5], 71), part)
    return dict(query_tokens=query_tokens, key_tokens=key_tokens, value_tokens=value_tokens, grad_out=grad_out, far_block=far_block)


def offsets_for(frame_count):
    distances = [2, 3]
    power_step = 4
    while power_step < frame_count:
        distances.append(power_step)
        power_step = power_step * 2
    return [sign_value * distance_step for distance_step in distances for sign_value in (1, -1)]


def far_window(entries, is_valid):
    pair_start = jnp.maximum(entries[0], 0).astype(jnp.int32)
    pair_index = jnp.arange(2, dtype=jnp.int32)
    far_hit = is_valid & (entries[:, None] >= 0) & ((entries[:, None] - pair_start) == pair_index[None, :])
    far_hit = jnp.repeat(jnp.repeat(far_hit, BLK, axis=0), BLK, axis=1)
    return pair_start, far_hit


def attend_parts(queries, grads_out, keys_all, visible):
    score_scale = HD ** -0.5
    key_part = keys_all[:, :HD]
    value_part = keys_all[:, HD:]
    scores = jnp.dot(queries, key_part.T, preferred_element_type=jnp.float32) * score_scale
    scores = jnp.where(visible, scores, -jnp.inf)
    row_max = jnp.max(scores, axis=1, keepdims=True)
    row_total = jnp.sum(jnp.exp(scores - row_max), axis=1, keepdims=True)
    log_total = row_max + jnp.log(row_total)
    weights = jnp.exp(scores - log_total).astype(jnp.bfloat16)
    out_rows = jnp.dot(weights, value_part, preferred_element_type=jnp.float32)
    row_delta = jnp.sum(out_rows * grads_out.astype(jnp.float32), axis=1, keepdims=True)
    dweights = jnp.dot(grads_out, value_part.T, preferred_element_type=jnp.float32)
    dscores = (weights.astype(jnp.float32) * (dweights - row_delta)).astype(jnp.bfloat16)
    query_rows_grad = jnp.dot(dscores, key_part, preferred_element_type=jnp.float32) * score_scale
    return out_rows, query_rows_grad, weights, dscores


def key_terms(weights, dscores, queries, grads_out):
    score_scale = HD ** -0.5
    key_side = jnp.dot(dscores.T, queries, preferred_element_type=jnp.float32) * score_scale
    value_side = jnp.dot(weights.T, grads_out, preferred_element_type=jnp.float32)
    return jnp.concatenate([key_side, value_side], axis=1)


def reference(query_tokens, key_tokens, value_tokens, grad_out, far_block):
    frame_count = FRAMES
    offsets = offsets_for(frame_count)
    joined = jnp.concatenate([key_tokens, value_tokens], axis=1)
    blank_rows = jnp.zeros((TOK_DEV, 2 * HD), jnp.bfloat16)
    padded = jnp.concatenate([blank_rows, joined, blank_rows], axis=0)
    frame_ids = jnp.arange(frame_count, dtype=jnp.int32)

    def one_frame(grad_acc, frame_index):
        begin_row = (frame_index * TOK_DEV).astype(jnp.int32)
        query_rows = lax.dynamic_slice_in_dim(query_tokens, begin_row, TOK_DEV, 0)
        dout_rows = lax.dynamic_slice_in_dim(grad_out, begin_row, TOK_DEV, 0)
        near_keys = lax.dynamic_slice_in_dim(padded, begin_row, 3 * TOK_DEV, 0)
        neighbour = frame_index + jnp.arange(3, dtype=jnp.int32) - 1
        near_ok = jnp.repeat((neighbour >= 0) & (neighbour < frame_count), TOK_DEV)
        pieces = [near_keys]
        mask_list = [jnp.broadcast_to(near_ok[None, :], (TOK_DEV, 3 * TOK_DEV))]
        start_rows = []
        for offset in offsets:
            other_frame = frame_index + offset
            is_valid = (other_frame >= 0) & (other_frame < frame_count)
            safe_frame = jnp.clip(other_frame, 0, frame_count - 1).astype(jnp.int32)
            entries = far_block[frame_index, safe_frame]
            pair_start, far_hit = far_window(entries, is_valid)
            row_begin = (safe_frame * TOK_DEV + pair_start * BLK).astype(jnp.int32)
            pieces.append(lax.dynamic_slice_in_dim(joined, row_begin, 2 * BLK, 0))
            mask_list.append(far_hit)
            start_rows.append(row_begin)
        keys_all = jnp.concatenate(pieces, axis=0)
        visible = jnp.concatenate(mask_list, axis=1)
        out_rows, query_rows_grad, weights, dscores = attend_parts(query_rows, dout_rows, keys_all, visible)
        grads = key_terms(weights, dscores, query_rows, dout_rows)
        current = lax.dynamic_slice_in_dim(grad_acc, begin_row, 3 * TOK_DEV, 0)
        grad_acc = lax.dynamic_update_slice_in_dim(grad_acc, current + grads[:3 * TOK_DEV], begin_row, 0)
        for slot_index in range(len(offsets)):
            row_begin = (start_rows[slot_index] + TOK_DEV).astype(jnp.int32)
            first_row = 3 * TOK_DEV + slot_index * 2 * BLK
            grad_piece = grads[first_row:first_row + 2 * BLK]
            current = lax.dynamic_slice_in_dim(grad_acc, row_begin, 2 * BLK, 0)
            grad_acc = lax.dynamic_update_slice_in_dim(grad_acc, current + grad_piece, row_begin, 0)
        return grad_acc, (out_rows, query_rows_grad)

    start_state = jnp.zeros(((frame_count + 2) * TOK_DEV, 2 * HD), jnp.float32)
    grad_acc, (out_all, query_all) = lax.scan(one_frame, start_state, frame_ids)
    grad_total = grad_acc[TOK_DEV:TOK_DEV + TOKENS]
    attention_out = out_all.reshape(TOKENS, HD)
    query_grad = query_all.reshape(TOKENS, HD)
    key_grad = grad_total[:, :HD]
    value_grad = grad_total[:, HD:]
    return (attention_out, query_grad, key_grad, value_grad)
```

```python
import jax
import jax.numpy as jnp
from jax import lax
from jax.sharding import PartitionSpec as P

HD = 128
BLK = 128


def offsets_for(frame_count):
    distances = [2, 3]
    power_step = 4
    while power_step < frame_count:
        distances.append(power_step)
        power_step = power_step * 2
    return [sign_value * distance_step for distance_step in distances for sign_value in (1, -1)]


def pieces_for(frame_count):
    half = frame_count // 2
    near = [(1, False), (-1, False)]
    far = []
    for offset in offsets_for(frame_count):
        if abs(offset) == half:
            if offset > 0:
                far.append((half, True))
        else:
            far.append((offset, False))
    return near, far


def receive(value, axis, shift, wrap):
    count = lax.axis_size(axis)
    if wrap:
        pairs = [(source, (source - shift) % count) for source in range(count)]
    else:
        pairs = [(source, source - shift) for source in range(count) if 0 <= source - shift < count]
    return lax.ppermute(value, axis, pairs)


def other_frame(device, shift, wrap, count):
    if wrap:
        return (device + shift) % count
    return device + shift


def shards(query_tokens, key_tokens, value_tokens, grad_out, far_block):
    rows = query_tokens.shape[0]
    blocks = rows // BLK
    count = lax.axis_size("seq")
    device = lax.axis_index("seq")
    scale = HD ** (-0.5)
    across = (((1,), (1,)), ((), ()))
    over_rows = (((0,), (0,)), ((), ()))
    near, far = pieces_for(count)

    pack = jnp.concatenate([key_tokens, value_tokens, query_tokens, grad_out], axis=1)
    got_near = [receive(pack, "seq", s, w) for s, w in near]
    got_far = [receive(pack, "seq", s, w) for s, w in far]

    near_frames = [other_frame(device, s, w, count) for s, w in near]
    far_frames = [other_frame(device, s, w, count) for s, w in far]
    near_ok = [(g >= 0) & (g < count) for g in near_frames]
    far_seen = []
    for g in far_frames:
        inside = (g >= 0) & (g < count)
        entries = far_block[device, jnp.clip(g, 0, count - 1)]
        far_seen.append([inside & (entries[b] >= 0) for b in range(blocks)])

    near_k = [key_tokens] + [p[:, :HD] for p in got_near]
    near_v = [value_tokens] + [p[:, HD : 2 * HD] for p in got_near]
    near_mask = [jnp.bool_(True)] + near_ok
    kn = jnp.concatenate(near_k, axis=0)
    vn = jnp.concatenate(near_v, axis=0)
    near_cols = jnp.concatenate(
        [jnp.broadcast_to(m, (rows,)) for m in near_mask], axis=0
    )

    outs, dqs, stats = [], [], []
    self_dk, self_dv = [], []
    for b in range(blocks):
        rs = slice(b * BLK, (b + 1) * BLK)
        qb = query_tokens[rs]
        dob = grad_out[rs]
        kf = jnp.concatenate([p[rs, :HD] for p in got_far], axis=0)
        vf = jnp.concatenate([p[rs, HD : 2 * HD] for p in got_far], axis=0)
        far_cols = jnp.concatenate(
            [jnp.broadcast_to(far_seen[i][b], (BLK,)) for i in range(len(far))], axis=0
        )
        k_all = jnp.concatenate([kn, kf], axis=0)
        v_all = jnp.concatenate([vn, vf], axis=0)
        cols = jnp.concatenate([near_cols, far_cols], axis=0)
        s = lax.dot_general(qb, k_all, across, preferred_element_type=jnp.float32) * scale
        s = jnp.where(cols[None, :], s, -jnp.inf)
        m = jnp.max(s, axis=1, keepdims=True)
        total = jnp.sum(jnp.exp(s - m), axis=1, keepdims=True)
        lse = m + jnp.log(total)
        w = jnp.exp(s - lse).astype(jnp.bfloat16)
        o = jnp.dot(w, v_all, preferred_element_type=jnp.float32)
        delta = jnp.sum(o * dob.astype(jnp.float32), axis=1, keepdims=True)
        dw = lax.dot_general(dob, v_all, across, preferred_element_type=jnp.float32)
        ds = (w.astype(jnp.float32) * (dw - delta)).astype(jnp.bfloat16)
        dq = jnp.dot(ds, k_all, preferred_element_type=jnp.float32) * scale
        outs.append(o)
        dqs.append(dq)
        stats.append(jnp.concatenate([lse[:, 0], delta[:, 0]], axis=0))
        self_dk.append(
            lax.dot_general(ds[:, :rows], qb, over_rows, preferred_element_type=jnp.float32)
        )
        self_dv.append(
            lax.dot_general(w[:, :rows], dob, over_rows, preferred_element_type=jnp.float32)
        )

    attention_out = jnp.concatenate(outs, axis=0)
    query_grad = jnp.concatenate(dqs, axis=0)
    stat_pack = jnp.concatenate(stats, axis=0).reshape(2 * blocks, BLK)
    stat_pack = jnp.concatenate(
        [stat_pack, jnp.zeros((8 - 2 * blocks, BLK), jnp.float32)], axis=0
    )

    got_near_stats = [receive(stat_pack, "seq", s, w) for s, w in near]
    got_far_stats = [receive(stat_pack, "seq", s, w) for s, w in far]

    dk_total = jnp.stack(self_dk, axis=0).sum(axis=0) * scale
    dv_total = jnp.stack(self_dv, axis=0).sum(axis=0)

    def key_terms(q_v, do_v, lse_v, delta_v, k_g, v_g, seen):
        s = lax.dot_general(q_v, k_g, across, preferred_element_type=jnp.float32) * scale
        s = jnp.where(seen, s, -jnp.inf)
        w = jnp.exp(s - lse_v[:, None]).astype(jnp.bfloat16)
        dw = lax.dot_general(do_v, v_g, across, preferred_element_type=jnp.float32)
        ds = (w.astype(jnp.float32) * (dw - delta_v[:, None])).astype(jnp.bfloat16)
        dk = lax.dot_general(ds, q_v, over_rows, preferred_element_type=jnp.float32)
        dv = lax.dot_general(w, do_v, over_rows, preferred_element_type=jnp.float32)
        return dk, dv

    def stat_rows(st):
        lse_v = jnp.concatenate([st[2 * b] for b in range(blocks)], axis=0)
        delta_v = jnp.concatenate([st[2 * b + 1] for b in range(blocks)], axis=0)
        return lse_v, delta_v

    for i in range(len(near)):
        p = got_near[i]
        lse_v, delta_v = stat_rows(got_near_stats[i])
        dk, dv = key_terms(
            p[:, 2 * HD : 3 * HD], p[:, 3 * HD :], lse_v, delta_v, key_tokens, value_tokens, near_ok[i]
        )
        dk_total = dk_total + dk * scale
        dv_total = dv_total + dv

    for i, (shift, wrap) in enumerate(far):
        p = got_far[i]
        st = got_far_stats[i]
        f = far_frames[i]
        inside = (f >= 0) & (f < count)
        entries = far_block[jnp.clip(f, 0, count - 1), device]
        dk_parts, dv_parts = [], []
        for b in range(blocks):
            rs = slice(b * BLK, (b + 1) * BLK)
            seen = inside & (entries[b] >= 0)
            dk, dv = key_terms(
                p[rs, 2 * HD : 3 * HD],
                p[rs, 3 * HD :],
                st[2 * b],
                st[2 * b + 1],
                key_tokens[rs],
                value_tokens[rs],
                seen,
            )
            dk_parts.append(dk)
            dv_parts.append(dv)
        dk_total = dk_total + jnp.concatenate(dk_parts, axis=0) * scale
        dv_total = dv_total + jnp.concatenate(dv_parts, axis=0)

    return (attention_out, query_grad, dk_total, dv_total)


def solution(mesh):
    return jax.shard_map(
        shards,
        mesh=mesh,
        in_specs=(P("seq", "head"), P("seq", "head"), P("seq", "head"), P("seq", "head"), P()),
        out_specs=(P("seq", "head"), P("seq", "head"), P("seq", "head"), P("seq", "head")),
        check_vma=False,
    )
```

```python
import jax
import jax.numpy as jnp
from jax import lax
from jax.sharding import PartitionSpec as P

HD = 128
BLK = 128


def offsets_for(frame_count):
    distances = [2, 3]
    power_step = 4
    while power_step < frame_count:
        distances.append(power_step)
        power_step = power_step * 2
    return [sign_value * distance_step for distance_step in distances for sign_value in (1, -1)]


def pieces_for(frame_count):
    half = frame_count // 2
    near = [(1, False), (-1, False)]
    far = []
    for offset in offsets_for(frame_count):
        if abs(offset) == half:
            if offset > 0:
                far.append((half, True))
        else:
            far.append((offset, False))
    return near, far


def receive(value, axis, shift, wrap):
    count = lax.axis_size(axis)
    if wrap:
        pairs = [(source, (source - shift) % count) for source in range(count)]
    else:
        pairs = [(source, source - shift) for source in range(count) if 0 <= source - shift < count]
    return lax.ppermute(value, axis, pairs)


def other_frame(device, shift, wrap, count):
    if wrap:
        return (device + shift) % count
    return device + shift


def shards(query_tokens, key_tokens, value_tokens, grad_out, far_block):
    rows = query_tokens.shape[0]
    blocks = rows // BLK
    count = lax.axis_size("seq")
    device = lax.axis_index("seq")
    scale = HD ** (-0.5)
    across = (((1,), (1,)), ((), ()))
    over_rows = (((0,), (0,)), ((), ()))
    near, far = pieces_for(count)

    pack = jnp.concatenate([key_tokens, value_tokens, query_tokens, grad_out], axis=1)
    got_near = [receive(pack, "seq", s, w) for s, w in near]
    got_far = [receive(pack, "seq", s, w) for s, w in far]

    near_frames = [other_frame(device, s, w, count) for s, w in near]
    far_frames = [other_frame(device, s, w, count) for s, w in far]
    near_ok = [(g >= 0) & (g < count) for g in near_frames]
    far_seen = []
    for g in far_frames:
        inside = (g >= 0) & (g < count)
        entries = far_block[device, jnp.clip(g, 0, count - 1)]
        far_seen.append([inside & (entries[b] >= 0) for b in range(blocks)])

    near_k = [key_tokens] + [p[:, :HD] for p in got_near]
    near_v = [value_tokens] + [p[:, HD : 2 * HD] for p in got_near]
    near_mask = [jnp.bool_(True)] + near_ok
    kn = jnp.concatenate(near_k, axis=0)
    vn = jnp.concatenate(near_v, axis=0)
    near_cols = jnp.concatenate(
        [jnp.broadcast_to(m, (rows,)) for m in near_mask], axis=0
    )

    outs, dqs, stats = [], [], []
    self_dk, self_dv = [], []
    for b in range(blocks):
        rs = slice(b * BLK, (b + 1) * BLK)
        qb = query_tokens[rs]
        dob = grad_out[rs]
        kf = jnp.concatenate([p[rs, :HD] for p in got_far], axis=0)
        vf = jnp.concatenate([p[rs, HD : 2 * HD] for p in got_far], axis=0)
        far_cols = jnp.concatenate(
            [jnp.broadcast_to(far_seen[i][b], (BLK,)) for i in range(len(far))], axis=0
        )
        k_all = jnp.concatenate([kn, kf], axis=0)
        v_all = jnp.concatenate([vn, vf], axis=0)
        cols = jnp.concatenate([near_cols, far_cols], axis=0)
        s = lax.dot_general(qb, k_all, across, preferred_element_type=jnp.float32) * scale
        s = jnp.where(cols[None, :], s, -jnp.inf)
        m = jnp.max(s, axis=1, keepdims=True)
        total = jnp.sum(jnp.exp(s - m), axis=1, keepdims=True)
        lse = m + jnp.log(total)
        w = jnp.exp(s - lse).astype(jnp.bfloat16)
        o = jnp.dot(w, v_all, preferred_element_type=jnp.float32)
        delta = jnp.sum(o * dob.astype(jnp.float32), axis=1, keepdims=True)
        dw = lax.dot_general(dob, v_all, across, preferred_element_type=jnp.float32)
        ds = (w.astype(jnp.float32) * (dw - delta)).astype(jnp.bfloat16)
        dq = jnp.dot(ds, k_all, preferred_element_type=jnp.float32) * scale
        outs.append(o)
        dqs.append(dq)
        stats.append(jnp.concatenate([lse[:, 0], delta[:, 0]], axis=0))
        self_dk.append(
            lax.dot_general(ds[:, :rows], qb, over_rows, preferred_element_type=jnp.float32)
        )
        self_dv.append(
            lax.dot_general(w[:, :rows], dob, over_rows, preferred_element_type=jnp.float32)
        )

    attention_out = jnp.concatenate(outs, axis=0)
    query_grad = jnp.concatenate(dqs, axis=0)
    stat_pack = jnp.concatenate(stats, axis=0).reshape(2 * blocks, BLK)
    stat_pack = jnp.concatenate(
        [stat_pack, jnp.zeros((8 - 2 * blocks, BLK), jnp.float32)], axis=0
    )

    all_stats = lax.all_gather(stat_pack, "seq")

    def stats_of(frame):
        return lax.dynamic_index_in_dim(all_stats, jnp.clip(frame, 0, count - 1), 0, keepdims=False)

    got_near_stats = [stats_of(g) for g in near_frames]
    got_far_stats = [stats_of(g) for g in far_frames]

    dk_total = jnp.stack(self_dk, axis=0).sum(axis=0) * scale
    dv_total = jnp.stack(self_dv, axis=0).sum(axis=0)

    def key_terms(q_v, do_v, lse_v, delta_v, k_g, v_g, seen):
        s = lax.dot_general(q_v, k_g, across, preferred_element_type=jnp.float32) * scale
        s = jnp.where(seen, s, -jnp.inf)
        w = jnp.exp(s - lse_v[:, None]).astype(jnp.bfloat16)
        dw = lax.dot_general(do_v, v_g, across, preferred_element_type=jnp.float32)
        ds = (w.astype(jnp.float32) * (dw - delta_v[:, None])).astype(jnp.bfloat16)
        dk = lax.dot_general(ds, q_v, over_rows, preferred_element_type=jnp.float32)
        dv = lax.dot_general(w, do_v, over_rows, preferred_element_type=jnp.float32)
        return dk, dv

    def stat_rows(st):
        lse_v = jnp.concatenate([st[2 * b] for b in range(blocks)], axis=0)
        delta_v = jnp.concatenate([st[2 * b + 1] for b in range(blocks)], axis=0)
        return lse_v, delta_v

    for i in range(len(near)):
        p = got_near[i]
        lse_v, delta_v = stat_rows(got_near_stats[i])
        dk, dv = key_terms(
            p[:, 2 * HD : 3 * HD], p[:, 3 * HD :], lse_v, delta_v, key_tokens, value_tokens, near_ok[i]
        )
        dk_total = dk_total + dk * scale
        dv_total = dv_total + dv

    for i, (shift, wrap) in enumerate(far):
        p = got_far[i]
        st = got_far_stats[i]
        f = far_frames[i]
        inside = (f >= 0) & (f < count)
        entries = far_block[jnp.clip(f, 0, count - 1), device]
        dk_parts, dv_parts = [], []
        for b in range(blocks):
            rs = slice(b * BLK, (b + 1) * BLK)
            seen = inside & (entries[b] >= 0)
            dk, dv = key_terms(
                p[rs, 2 * HD : 3 * HD],
                p[rs, 3 * HD :],
                st[2 * b],
                st[2 * b + 1],
                key_tokens[rs],
                value_tokens[rs],
                seen,
            )
            dk_parts.append(dk)
            dv_parts.append(dv)
        dk_total = dk_total + jnp.concatenate(dk_parts, axis=0) * scale
        dv_total = dv_total + jnp.concatenate(dv_parts, axis=0)

    return (attention_out, query_grad, dk_total, dv_total)


def solution(mesh):
    return jax.shard_map(
        shards,
        mesh=mesh,
        in_specs=(P("seq", "head"), P("seq", "head"), P("seq", "head"), P("seq", "head"), P()),
        out_specs=(P("seq", "head"), P("seq", "head"), P("seq", "head"), P("seq", "head")),
        check_vma=False,
    )
```

```python
import jax
import jax.numpy as jnp
from jax import lax
from jax.sharding import PartitionSpec as P

HD = 128
BLK = 128


def extended(shard, sides, width):
    for axis, dim in sides:
        size, length = (lax.axis_size(axis), shard.shape[dim])
        up = [(i, (i + 1) % size) for i in range(size - 1)]
        down = [(j, i) for i, j in up]
        last = lax.slice_in_dim(shard, length - width, length, axis=dim)
        leading = lax.slice_in_dim(shard, 0, width, axis=dim)
        before = lax.ppermute(last, axis, up)
        after = lax.ppermute(leading, axis, down)
        shard = jnp.concatenate([before, shard, after], axis=dim)
    return shard


def from_behind(value, axis, steps):
    count = lax.axis_size(axis)
    leading, last = (max(0, -steps), min(count, count - steps))
    return lax.ppermute(value, axis, [(source, source + steps) for source in range(leading, last)])


def offsets_for(frame_count):
    distances = [2, 3]
    power_step = 4
    while power_step < frame_count:
        distances.append(power_step)
        power_step = power_step * 2
    return [sign_value * distance_step for distance_step in distances for sign_value in (1, -1)]


def far_window(entries, is_valid):
    pair_start = jnp.maximum(entries[0], 0)
    pair_index = jnp.arange(2, dtype=jnp.int32)
    far_hit = (
        is_valid & (entries[:, None] >= 0) & (entries[:, None] - pair_start == pair_index[None, :])
    )
    far_hit = jnp.repeat(jnp.repeat(far_hit, BLK, axis=0), BLK, axis=1)
    return (pair_start, far_hit)


def attend_parts(queries, grads_out, keys_all, visible):
    score_scale = HD ** (-0.5)
    across = (((1,), (1,)), ((), ()))
    key_part = keys_all[:, :HD]
    value_part = keys_all[:, HD:]
    scores = (
        lax.dot_general(queries, key_part, across, preferred_element_type=jnp.float32) * score_scale
    )
    scores = jnp.where(visible, scores, -jnp.inf)
    row_max = jnp.max(scores, axis=1, keepdims=True)
    row_total = jnp.sum(jnp.exp(scores - row_max), axis=1, keepdims=True)
    log_total = row_max + jnp.log(row_total)
    weights = jnp.exp(scores - log_total).astype(jnp.bfloat16)
    out_rows = jnp.dot(weights, value_part, preferred_element_type=jnp.float32)
    row_delta = jnp.sum(out_rows * grads_out.astype(jnp.float32), axis=1, keepdims=True)
    dweights = lax.dot_general(grads_out, value_part, across, preferred_element_type=jnp.float32)
    dscores = (weights.astype(jnp.float32) * (dweights - row_delta)).astype(jnp.bfloat16)
    query_rows_grad = jnp.dot(dscores, key_part, preferred_element_type=jnp.float32) * score_scale
    return (out_rows, query_rows_grad, weights, dscores, log_total, row_delta)


def key_terms(weights, dscores, queries, grads_out):
    score_scale = HD ** (-0.5)
    over_rows = (((0,), (0,)), ((), ()))
    key_side = (
        lax.dot_general(dscores, queries, over_rows, preferred_element_type=jnp.float32)
        * score_scale
    )
    value_side = lax.dot_general(weights, grads_out, over_rows, preferred_element_type=jnp.float32)
    return jnp.concatenate([key_side, value_side], axis=1)


def shards(query_tokens, key_tokens, value_tokens, grad_out, far_block):
    tok_rows = query_tokens.shape[0]
    frame_count = lax.axis_size("seq")
    device = lax.axis_index("seq")
    offsets = offsets_for(frame_count)
    joined = jnp.concatenate([key_tokens, value_tokens], axis=1)
    near_keys = extended(joined, (("seq", 0),), tok_rows)
    neighbour = device + jnp.arange(3, dtype=jnp.int32) - 1
    near_ok = jnp.repeat((neighbour >= 0) & (neighbour < frame_count), tok_rows)
    pieces = [near_keys]
    mask_list = [jnp.broadcast_to(near_ok[None, :], (tok_rows, 3 * tok_rows))]
    half = frame_count // 2
    offsets = [o for o in offsets if o != -half]
    for offset in offsets:
        if offset == half:
            arrived = lax.ppermute(
                joined, "seq", [(src, (src + half) % frame_count) for src in range(frame_count)]
            )
            other_frame = (device + half) % frame_count
        else:
            arrived = from_behind(joined, "seq", -offset)
            other_frame = device + offset
        is_valid = (other_frame >= 0) & (other_frame < frame_count)
        safe_frame = jnp.clip(other_frame, 0, frame_count - 1)
        entries = far_block[device, safe_frame]
        pair_start, far_hit = far_window(entries, is_valid)
        pieces.append(arrived)
        mask_list.append(far_hit)
    keys_all = jnp.concatenate(pieces, axis=0)
    visible = jnp.concatenate(mask_list, axis=1)
    attention_out, query_grad, weights, dscores, log_total, row_delta = attend_parts(
        query_tokens, grad_out, keys_all, visible
    )
    near_terms = key_terms(
        weights[:, : 3 * tok_rows], dscores[:, : 3 * tok_rows], query_tokens, grad_out
    )
    sent = near_terms.astype(jnp.bfloat16)
    from_after = from_behind(sent[:tok_rows], "seq", -1).astype(jnp.float32)
    from_before = from_behind(sent[2 * tok_rows :], "seq", 1).astype(jnp.float32)
    grad_total = near_terms[tok_rows : 2 * tok_rows] + from_after + from_before
    far_terms = key_terms(
        weights[:, 3 * tok_rows :], dscores[:, 3 * tok_rows :], query_tokens, grad_out
    )
    for slot_index in range(len(offsets)):
        first_row = slot_index * 2 * BLK
        grad_piece = far_terms[first_row : first_row + 2 * BLK].astype(jnp.bfloat16)
        if offsets[slot_index] == half:
            returned = lax.ppermute(
                grad_piece, "seq", [(src, (src + half) % frame_count) for src in range(frame_count)]
            )
        else:
            returned = from_behind(grad_piece, "seq", offsets[slot_index])
        returned = returned.astype(jnp.float32)
        current = grad_total
        grad_total = current + returned
    key_grad = grad_total[:, :HD]
    value_grad = grad_total[:, HD:]
    return (attention_out, query_grad, key_grad, value_grad)


def solution(mesh):
    return jax.shard_map(
        shards,
        mesh=mesh,
        in_specs=(P("seq", "head"), P("seq", "head"), P("seq", "head"), P("seq", "head"), P()),
        out_specs=(P("seq", "head"), P("seq", "head"), P("seq", "head"), P("seq", "head")),
        check_vma=False,
    )
```

```python
import jax
import jax.numpy as jnp
import numpy as np
from jax import lax
from jax.sharding import Mesh
from jax.sharding import PartitionSpec as P

HD = 128
BLK = 128
ROW = 16
ROW_AXES = ("z", "c")


def offsets_for(frame_count):
    distances = [2, 3]
    power_step = 4
    while power_step < frame_count:
        distances.append(power_step)
        power_step = power_step * 2
    return [sign_value * distance_step for distance_step in distances for sign_value in (1, -1)]


def far_window(entries, is_valid):
    pair_start = jnp.maximum(entries[0], 0)
    pair_index = jnp.arange(2, dtype=jnp.int32)
    far_hit = (
        is_valid & (entries[:, None] >= 0) & (entries[:, None] - pair_start == pair_index[None, :])
    )
    far_hit = jnp.repeat(jnp.repeat(far_hit, BLK, axis=0), BLK, axis=1)
    return (pair_start, far_hit)


def attend_parts(queries, grads_out, keys_all, visible):
    score_scale = HD ** (-0.5)
    across = (((1,), (1,)), ((), ()))
    key_part = keys_all[:, :HD]
    value_part = keys_all[:, HD:]
    scores = (
        lax.dot_general(queries, key_part, across, preferred_element_type=jnp.float32) * score_scale
    )
    scores = jnp.where(visible, scores, -jnp.inf)
    row_max = jnp.max(scores, axis=1, keepdims=True)
    row_total = jnp.sum(jnp.exp(scores - row_max), axis=1, keepdims=True)
    log_total = row_max + jnp.log(row_total)
    weights = jnp.exp(scores - log_total).astype(jnp.bfloat16)
    out_rows = jnp.dot(weights, value_part, preferred_element_type=jnp.float32)
    row_delta = jnp.sum(out_rows * grads_out.astype(jnp.float32), axis=1, keepdims=True)
    dweights = lax.dot_general(grads_out, value_part, across, preferred_element_type=jnp.float32)
    dscores = (weights.astype(jnp.float32) * (dweights - row_delta)).astype(jnp.bfloat16)
    query_rows_grad = jnp.dot(dscores, key_part, preferred_element_type=jnp.float32) * score_scale
    return (out_rows, query_rows_grad, weights, dscores)


def key_terms(weights, dscores, queries, grads_out):
    score_scale = HD ** (-0.5)
    over_rows = (((0,), (0,)), ((), ()))
    key_side = (
        lax.dot_general(dscores, queries, over_rows, preferred_element_type=jnp.float32)
        * score_scale
    )
    value_side = lax.dot_general(weights, grads_out, over_rows, preferred_element_type=jnp.float32)
    return jnp.concatenate([key_side, value_side], axis=1)


def swap_pairs(frame_count):
    half = ROW // 2
    pairs = []
    for source in range(frame_count):
        target = source - half if source % ROW < half else source + half
        if 0 <= target < frame_count:
            pairs.append((source, target))
    return pairs


def shards(query_tokens, key_tokens, value_tokens, grad_out, far_block):
    tok_rows = query_tokens.shape[0]
    cols = lax.axis_size("y")
    frame_count = cols * ROW
    half = ROW // 2
    y = lax.axis_index("y")
    w = lax.axis_index("z") * lax.axis_size("c") + lax.axis_index("c")
    device = y * ROW + w
    offsets = offsets_for(frame_count)
    seq_axes = ("y",) + ROW_AXES

    joined = jnp.concatenate([key_tokens, value_tokens], axis=1)
    own_row = lax.all_gather(joined, ROW_AXES)
    swapped = lax.ppermute(joined, seq_axes, swap_pairs(frame_count))
    near_rows = lax.all_gather(swapped, ROW_AXES)
    column = lax.all_gather(joined, "y")
    table = jnp.concatenate([near_rows[:half], own_row, near_rows[half:]], axis=0)

    def row_frame(offset):
        index = jnp.clip(w + offset + half, 0, 2 * ROW - 1)
        return lax.dynamic_index_in_dim(table, index, 0, keepdims=False)

    def column_frame(offset):
        index = jnp.clip(y + offset // ROW, 0, cols - 1)
        return lax.dynamic_index_in_dim(column, index, 0, keepdims=False)

    def fetch(offset):
        return row_frame(offset) if abs(offset) <= half else column_frame(offset)

    near_keys = jnp.concatenate([row_frame(-1), joined, row_frame(1)], axis=0)
    neighbour = device + jnp.arange(3, dtype=jnp.int32) - 1
    near_ok = jnp.repeat((neighbour >= 0) & (neighbour < frame_count), tok_rows)
    pieces = [near_keys]
    mask_list = [jnp.broadcast_to(near_ok[None, :], (tok_rows, 3 * tok_rows))]
    for offset in offsets:
        arrived = fetch(offset)
        other_frame = device + offset
        is_valid = (other_frame >= 0) & (other_frame < frame_count)
        safe_frame = jnp.clip(other_frame, 0, frame_count - 1)
        entries = far_block[device, safe_frame]
        pair_start, far_hit = far_window(entries, is_valid)
        pieces.append(arrived)
        mask_list.append(far_hit)
    keys_all = jnp.concatenate(pieces, axis=0)
    visible = jnp.concatenate(mask_list, axis=1)
    attention_out, query_grad, weights, dscores = attend_parts(
        query_tokens, grad_out, keys_all, visible
    )
    terms = key_terms(weights, dscores, query_tokens, grad_out)

    near_table = jnp.zeros((2 * ROW,) + joined.shape, jnp.float32)
    far_column = jnp.zeros((cols,) + joined.shape, jnp.float32)
    term_offsets = [-1, 1] + offsets
    term_rows = [0, 2 * tok_rows] + [(3 + i) * tok_rows for i in range(len(offsets))]
    for offset, first in zip(term_offsets, term_rows):
        piece = terms[first : first + tok_rows]
        if abs(offset) <= half:
            index = jnp.clip(w + offset + half, 0, 2 * ROW - 1)
            current = lax.dynamic_index_in_dim(near_table, index, 0, keepdims=True)
            near_table = lax.dynamic_update_index_in_dim(near_table, current + piece[None], index, 0)
        else:
            index = jnp.clip(y + offset // ROW, 0, cols - 1)
            current = lax.dynamic_index_in_dim(far_column, index, 0, keepdims=True)
            far_column = lax.dynamic_update_index_in_dim(far_column, current + piece[None], index, 0)
    own_sum = lax.psum_scatter(near_table[half : half + ROW], ROW_AXES, scatter_dimension=0)
    side = jnp.concatenate([near_table[:half], near_table[half + ROW :]], axis=0)
    side_sum = lax.psum_scatter(side, ROW_AXES, scatter_dimension=0)
    side_back = lax.ppermute(side_sum, seq_axes, swap_pairs(frame_count))
    column_sum = lax.psum_scatter(far_column, "y", scatter_dimension=0)
    grad_total = terms[tok_rows : 2 * tok_rows] + own_sum + side_back + column_sum
    key_grad = grad_total[:, :HD]
    value_grad = grad_total[:, HD:]
    return (attention_out, query_grad, key_grad, value_grad)


def solution(mesh):
    seq_count, head_count = mesh.devices.shape
    cols = seq_count // ROW
    devices = np.asarray(mesh.devices).reshape(cols, ROW // 2, 2, head_count)
    grid = Mesh(devices, ("y",) + ROW_AXES + ("head",))
    seq = ("y",) + ROW_AXES
    return jax.shard_map(
        shards,
        mesh=grid,
        in_specs=(P(seq, "head"), P(seq, "head"), P(seq, "head"), P(seq, "head"), P()),
        out_specs=(P(seq, "head"), P(seq, "head"), P(seq, "head"), P(seq, "head")),
        check_vma=False,
    )
```

```python
import jax
import jax.numpy as jnp
from jax import lax
from jax.sharding import PartitionSpec as P

HD = 128
BLK = 128


def extended(shard, sides, width):
    for axis, dim in sides:
        size, length = (lax.axis_size(axis), shard.shape[dim])
        up = [(i, (i + 1) % size) for i in range(size - 1)]
        down = [(j, i) for i, j in up]
        last = lax.slice_in_dim(shard, length - width, length, axis=dim)
        leading = lax.slice_in_dim(shard, 0, width, axis=dim)
        before = lax.ppermute(last, axis, up)
        after = lax.ppermute(leading, axis, down)
        shard = jnp.concatenate([before, shard, after], axis=dim)
    return shard


def from_behind(value, axis, steps):
    count = lax.axis_size(axis)
    leading, last = (max(0, -steps), min(count, count - steps))
    return lax.ppermute(value, axis, [(source, source + steps) for source in range(leading, last)])


def offsets_for(frame_count):
    distances = [2, 3]
    power_step = 4
    while power_step < frame_count:
        distances.append(power_step)
        power_step = power_step * 2
    return [sign_value * distance_step for distance_step in distances for sign_value in (1, -1)]


def far_window(entries, is_valid):
    pair_start = jnp.maximum(entries[0], 0)
    pair_index = jnp.arange(2, dtype=jnp.int32)
    far_hit = (
        is_valid & (entries[:, None] >= 0) & (entries[:, None] - pair_start == pair_index[None, :])
    )
    far_hit = jnp.repeat(jnp.repeat(far_hit, BLK, axis=0), BLK, axis=1)
    return (pair_start, far_hit)


def attend_parts(queries, grads_out, keys_all, visible):
    score_scale = HD ** (-0.5)
    across = (((1,), (1,)), ((), ()))
    key_part = keys_all[:, :HD]
    value_part = keys_all[:, HD:]
    scores = (
        lax.dot_general(queries, key_part, across, preferred_element_type=jnp.float32) * score_scale
    )
    scores = jnp.where(visible, scores, -jnp.inf)
    row_max = jnp.max(scores, axis=1, keepdims=True)
    row_total = jnp.sum(jnp.exp(scores - row_max), axis=1, keepdims=True)
    log_total = row_max + jnp.log(row_total)
    weights = jnp.exp(scores - log_total).astype(jnp.bfloat16)
    out_rows = jnp.dot(weights, value_part, preferred_element_type=jnp.float32)
    row_delta = jnp.sum(out_rows * grads_out.astype(jnp.float32), axis=1, keepdims=True)
    dweights = lax.dot_general(grads_out, value_part, across, preferred_element_type=jnp.float32)
    dscores = (weights.astype(jnp.float32) * (dweights - row_delta)).astype(jnp.bfloat16)
    query_rows_grad = jnp.dot(dscores, key_part, preferred_element_type=jnp.float32) * score_scale
    return (out_rows, query_rows_grad, weights, dscores, log_total, row_delta)


def key_terms(weights, dscores, queries, grads_out):
    score_scale = HD ** (-0.5)
    over_rows = (((0,), (0,)), ((), ()))
    key_side = (
        lax.dot_general(dscores, queries, over_rows, preferred_element_type=jnp.float32)
        * score_scale
    )
    value_side = lax.dot_general(weights, grads_out, over_rows, preferred_element_type=jnp.float32)
    return jnp.concatenate([key_side, value_side], axis=1)


RELAY = (
    (1, (0,)),
    (-8, (0,)),
    (16, (0,)),
    (2, (0, 1)),
    (-32, (0, 16)),
    (-4, (0, 1, 2, 3)),
    (64, (0, -32)),
    (8, (0, -4)),
)


def cyclic(value, axis, shift):
    count = lax.axis_size(axis)
    return lax.ppermute(value, axis, [(source, (source - shift) % count) for source in range(count)])


def relay_gather(own, axis):
    rows = own.shape[0]
    held = {0: own}
    for shift, sent in RELAY:
        got = cyclic(jnp.concatenate([held[e] for e in sent], axis=0), axis, shift)
        for j, e in enumerate(sent):
            held[e + shift] = got[j * rows : (j + 1) * rows]
    return held


def relay_return(terms, axis):
    acc = dict(terms)
    rows = acc[0].shape[0]
    for shift, sent in reversed(RELAY):
        buf = jnp.concatenate([acc.pop(e + shift).astype(jnp.bfloat16) for e in sent], axis=0)
        got = cyclic(buf, axis, -shift).astype(jnp.float32)
        for j, e in enumerate(sent):
            part = got[j * rows : (j + 1) * rows]
            acc[e] = acc[e] + part if e in acc else part
    return acc[0]


def shards(query_tokens, key_tokens, value_tokens, grad_out, far_block):
    tok_rows = query_tokens.shape[0]
    frame_count = lax.axis_size("seq")
    device = lax.axis_index("seq")
    offsets = offsets_for(frame_count)
    joined = jnp.concatenate([key_tokens, value_tokens], axis=1)
    held = relay_gather(joined, "seq")
    near_keys = jnp.concatenate([held[-1], joined, held[1]], axis=0)
    neighbour = device + jnp.arange(3, dtype=jnp.int32) - 1
    near_ok = jnp.repeat((neighbour >= 0) & (neighbour < frame_count), tok_rows)
    pieces = [near_keys]
    mask_list = [jnp.broadcast_to(near_ok[None, :], (tok_rows, 3 * tok_rows))]
    half = frame_count // 2
    offsets = [o for o in offsets if o != -half]
    for offset in offsets:
        arrived = held[offset]
        if offset == half:
            other_frame = (device + half) % frame_count
        else:
            other_frame = device + offset
        is_valid = (other_frame >= 0) & (other_frame < frame_count)
        safe_frame = jnp.clip(other_frame, 0, frame_count - 1)
        entries = far_block[device, safe_frame]
        pair_start, far_hit = far_window(entries, is_valid)
        pieces.append(arrived)
        mask_list.append(far_hit)
    keys_all = jnp.concatenate(pieces, axis=0)
    visible = jnp.concatenate(mask_list, axis=1)
    attention_out, query_grad, weights, dscores, log_total, row_delta = attend_parts(
        query_tokens, grad_out, keys_all, visible
    )
    terms = key_terms(weights, dscores, query_tokens, grad_out)
    by_offset = {
        -1: terms[:tok_rows],
        0: terms[tok_rows : 2 * tok_rows],
        1: terms[2 * tok_rows : 3 * tok_rows],
    }
    for slot_index, offset in enumerate(offsets):
        first_row = (3 + slot_index) * tok_rows
        by_offset[offset] = terms[first_row : first_row + tok_rows]
    grad_total = relay_return(by_offset, "seq")
    key_grad = grad_total[:, :HD]
    value_grad = grad_total[:, HD:]
    return (attention_out, query_grad, key_grad, value_grad)


def solution(mesh):
    return jax.shard_map(
        shards,
        mesh=mesh,
        in_specs=(P("seq", "head"), P("seq", "head"), P("seq", "head"), P("seq", "head"), P()),
        out_specs=(P("seq", "head"), P("seq", "head"), P("seq", "head"), P("seq", "head")),
        check_vma=False,
    )
```

```python
import jax
import jax.numpy as jnp
from jax import lax
from jax.sharding import PartitionSpec as P

HD = 128
BLK = 128


def extended(shard, sides, width):
    for axis, dim in sides:
        size, length = (lax.axis_size(axis), shard.shape[dim])
        up = [(i, (i + 1) % size) for i in range(size - 1)]
        down = [(j, i) for i, j in up]
        last = lax.slice_in_dim(shard, length - width, length, axis=dim)
        leading = lax.slice_in_dim(shard, 0, width, axis=dim)
        before = lax.ppermute(last, axis, up)
        after = lax.ppermute(leading, axis, down)
        shard = jnp.concatenate([before, shard, after], axis=dim)
    return shard


def from_behind(value, axis, steps):
    count = lax.axis_size(axis)
    leading, last = (max(0, -steps), min(count, count - steps))
    return lax.ppermute(value, axis, [(source, source + steps) for source in range(leading, last)])


def offsets_for(frame_count):
    distances = [2, 3]
    power_step = 4
    while power_step < frame_count:
        distances.append(power_step)
        power_step = power_step * 2
    return [sign_value * distance_step for distance_step in distances for sign_value in (1, -1)]


def far_window(entries, is_valid):
    pair_start = jnp.maximum(entries[0], 0)
    pair_index = jnp.arange(2, dtype=jnp.int32)
    far_hit = (
        is_valid & (entries[:, None] >= 0) & (entries[:, None] - pair_start == pair_index[None, :])
    )
    far_hit = jnp.repeat(jnp.repeat(far_hit, BLK, axis=0), BLK, axis=1)
    return (pair_start, far_hit)


def attend_parts(queries, grads_out, keys_all, visible):
    score_scale = HD ** (-0.5)
    across = (((1,), (1,)), ((), ()))
    key_part = keys_all[:, :HD]
    value_part = keys_all[:, HD:]
    scores = (
        lax.dot_general(queries, key_part, across, preferred_element_type=jnp.float32) * score_scale
    )
    scores = jnp.where(visible, scores, -jnp.inf)
    row_max = jnp.max(scores, axis=1, keepdims=True)
    row_total = jnp.sum(jnp.exp(scores - row_max), axis=1, keepdims=True)
    log_total = row_max + jnp.log(row_total)
    weights = jnp.exp(scores - log_total).astype(jnp.bfloat16)
    out_rows = jnp.dot(weights, value_part, preferred_element_type=jnp.float32)
    row_delta = jnp.sum(out_rows * grads_out.astype(jnp.float32), axis=1, keepdims=True)
    dweights = lax.dot_general(grads_out, value_part, across, preferred_element_type=jnp.float32)
    dscores = (weights.astype(jnp.float32) * (dweights - row_delta)).astype(jnp.bfloat16)
    query_rows_grad = jnp.dot(dscores, key_part, preferred_element_type=jnp.float32) * score_scale
    return (out_rows, query_rows_grad, weights, dscores, log_total, row_delta)


def key_terms(weights, dscores, queries, grads_out):
    score_scale = HD ** (-0.5)
    over_rows = (((0,), (0,)), ((), ()))
    key_side = (
        lax.dot_general(dscores, queries, over_rows, preferred_element_type=jnp.float32)
        * score_scale
    )
    value_side = lax.dot_general(weights, grads_out, over_rows, preferred_element_type=jnp.float32)
    return jnp.concatenate([key_side, value_side], axis=1)


def shards(query_tokens, key_tokens, value_tokens, grad_out, far_block):
    tok_rows = query_tokens.shape[0]
    frame_count = lax.axis_size("seq")
    device = lax.axis_index("seq")
    offsets = offsets_for(frame_count)
    joined = jnp.concatenate([key_tokens, value_tokens], axis=1)
    near_keys = extended(joined, (("seq", 0),), tok_rows)
    neighbour = device + jnp.arange(3, dtype=jnp.int32) - 1
    near_ok = (neighbour >= 0) & (neighbour < frame_count)
    pieces = [near_keys]
    half = frame_count // 2
    offsets = [o for o in offsets if o != -half]
    for offset in offsets:
        if offset == half:
            arrived = lax.ppermute(
                joined, "seq", [(src, (src + half) % frame_count) for src in range(frame_count)]
            )
        else:
            arrived = from_behind(joined, "seq", -offset)
        pieces.append(arrived)
    shifts = jnp.asarray(offsets, jnp.int32)
    other_frame = jnp.where(shifts == half, (device + half) % frame_count, device + shifts)
    is_valid = (other_frame >= 0) & (other_frame < frame_count)
    frame_rows = lax.dynamic_index_in_dim(far_block, device, 0, keepdims=False)
    entries = jnp.take(frame_rows, jnp.clip(other_frame, 0, frame_count - 1), axis=0)
    seen = is_valid[:, None] & (entries >= 0)
    blocks = tok_rows // BLK
    row_block = jnp.arange(tok_rows, dtype=jnp.int32) // BLK
    near_mask = jnp.broadcast_to(
        near_ok[None, :, None], (tok_rows, 3, tok_rows)
    ).reshape(tok_rows, 3 * tok_rows)
    seen_rows = jnp.take(seen, row_block, axis=1)
    diag = row_block[:, None] == row_block[None, :]
    far_mask = (diag[:, None, :] & seen_rows.T[:, :, None]).reshape(
        tok_rows, len(offsets) * tok_rows
    )
    keys_all = jnp.concatenate(pieces, axis=0)
    visible = jnp.concatenate([near_mask, far_mask], axis=1)
    attention_out, query_grad, weights, dscores, log_total, row_delta = attend_parts(
        query_tokens, grad_out, keys_all, visible
    )
    near_terms = key_terms(
        weights[:, : 3 * tok_rows], dscores[:, : 3 * tok_rows], query_tokens, grad_out
    )
    sent = near_terms.astype(jnp.bfloat16)
    from_after = from_behind(sent[:tok_rows], "seq", -1).astype(jnp.float32)
    from_before = from_behind(sent[2 * tok_rows :], "seq", 1).astype(jnp.float32)
    grad_total = near_terms[tok_rows : 2 * tok_rows] + from_after + from_before
    far_terms = key_terms(
        weights[:, 3 * tok_rows :], dscores[:, 3 * tok_rows :], query_tokens, grad_out
    )
    for slot_index in range(len(offsets)):
        first_row = slot_index * 2 * BLK
        grad_piece = far_terms[first_row : first_row + 2 * BLK].astype(jnp.bfloat16)
        if offsets[slot_index] == half:
            returned = lax.ppermute(
                grad_piece, "seq", [(src, (src + half) % frame_count) for src in range(frame_count)]
            )
        else:
            returned = from_behind(grad_piece, "seq", offsets[slot_index])
        returned = returned.astype(jnp.float32)
        current = grad_total
        grad_total = current + returned
    key_grad = grad_total[:, :HD]
    value_grad = grad_total[:, HD:]
    return (attention_out, query_grad, key_grad, value_grad)


def solution(mesh):
    return jax.shard_map(
        shards,
        mesh=mesh,
        in_specs=(P("seq", "head"), P("seq", "head"), P("seq", "head"), P("seq", "head"), P()),
        out_specs=(P("seq", "head"), P("seq", "head"), P("seq", "head"), P("seq", "head")),
        check_vma=False,
    )
```

```python
import jax
import jax.numpy as jnp
from jax import lax
from jax.sharding import PartitionSpec as P

HD = 128
BLK = 128


def extended(shard, sides, width):
    for axis, dim in sides:
        size, length = (lax.axis_size(axis), shard.shape[dim])
        up = [(i, (i + 1) % size) for i in range(size - 1)]
        down = [(j, i) for i, j in up]
        last = lax.slice_in_dim(shard, length - width, length, axis=dim)
        leading = lax.slice_in_dim(shard, 0, width, axis=dim)
        before = lax.ppermute(last, axis, up)
        after = lax.ppermute(leading, axis, down)
        shard = jnp.concatenate([before, shard, after], axis=dim)
    return shard


def from_behind(value, axis, steps):
    count = lax.axis_size(axis)
    leading, last = (max(0, -steps), min(count, count - steps))
    return lax.ppermute(value, axis, [(source, source + steps) for source in range(leading, last)])


def offsets_for(frame_count):
    distances = [2, 3]
    power_step = 4
    while power_step < frame_count:
        distances.append(power_step)
        power_step = power_step * 2
    return [sign_value * distance_step for distance_step in distances for sign_value in (1, -1)]


def far_window(entries, is_valid):
    pair_start = jnp.maximum(entries[0], 0)
    pair_index = jnp.arange(2, dtype=jnp.int32)
    far_hit = (
        is_valid & (entries[:, None] >= 0) & (entries[:, None] - pair_start == pair_index[None, :])
    )
    far_hit = jnp.repeat(jnp.repeat(far_hit, BLK, axis=0), BLK, axis=1)
    return (pair_start, far_hit)


def attend_parts(queries, grads_out, keys_all, visible):
    score_scale = HD ** (-0.5)
    across = (((1,), (1,)), ((), ()))
    key_part = keys_all[:, :HD]
    value_part = keys_all[:, HD:]
    scores = (
        lax.dot_general(queries, key_part, across, preferred_element_type=jnp.float32) * score_scale
    )
    scores = jnp.where(visible, scores, -jnp.inf)
    row_max = jnp.max(scores, axis=1, keepdims=True)
    row_total = jnp.sum(jnp.exp(scores - row_max), axis=1, keepdims=True)
    log_total = row_max + jnp.log(row_total)
    weights = jnp.exp(scores - log_total).astype(jnp.bfloat16)
    out_rows = jnp.dot(weights, value_part, preferred_element_type=jnp.float32)
    row_delta = jnp.sum(out_rows * grads_out.astype(jnp.float32), axis=1, keepdims=True)
    dweights = lax.dot_general(grads_out, value_part, across, preferred_element_type=jnp.float32)
    dscores = (weights.astype(jnp.float32) * (dweights - row_delta)).astype(jnp.bfloat16)
    query_rows_grad = jnp.dot(dscores, key_part, preferred_element_type=jnp.float32) * score_scale
    return (out_rows, query_rows_grad, weights, dscores, log_total, row_delta)


def key_terms(weights, dscores, queries, grads_out):
    score_scale = HD ** (-0.5)
    over_rows = (((0,), (0,)), ((), ()))
    key_side = (
        lax.dot_general(dscores, queries, over_rows, preferred_element_type=jnp.float32)
        * score_scale
    )
    value_side = lax.dot_general(weights, grads_out, over_rows, preferred_element_type=jnp.float32)
    return jnp.concatenate([key_side, value_side], axis=1)


def shards(query_tokens, key_tokens, value_tokens, grad_out, far_block):
    tok_rows = query_tokens.shape[0]
    frame_count = lax.axis_size("seq")
    device = lax.axis_index("seq")
    offsets = offsets_for(frame_count)
    joined = jnp.concatenate([key_tokens, value_tokens], axis=1)
    near_keys = extended(joined, (("seq", 0),), tok_rows)
    neighbour = device + jnp.arange(3, dtype=jnp.int32) - 1
    near_ok = (neighbour >= 0) & (neighbour < frame_count)
    pieces = [near_keys]
    half = frame_count // 2
    offsets = [o for o in offsets if o != -half]
    for offset in offsets:
        if offset == half:
            arrived = lax.ppermute(
                joined, "seq", [(src, (src + half) % frame_count) for src in range(frame_count)]
            )
        else:
            arrived = from_behind(joined, "seq", -offset)
        pieces.append(arrived)
    shifts = jnp.asarray(offsets, jnp.int32)
    other_frame = jnp.where(shifts == half, (device + half) % frame_count, device + shifts)
    is_valid = (other_frame >= 0) & (other_frame < frame_count)
    frame_rows = lax.dynamic_index_in_dim(far_block, device, 0, keepdims=False)
    entries = jnp.take(frame_rows, jnp.clip(other_frame, 0, frame_count - 1), axis=0)
    seen = is_valid[:, None] & (entries >= 0)
    blocks = tok_rows // BLK
    near_mask = jnp.broadcast_to(
        near_ok[None, :, None], (tok_rows, 3, tok_rows)
    ).reshape(tok_rows, 3 * tok_rows)
    near_keys_all = pieces[0]
    far_pieces = pieces[1:]
    outs, dqs, near_parts, far_parts = [], [], [], []
    for blk in range(blocks):
        rs = slice(blk * BLK, (blk + 1) * BLK)
        kv = jnp.concatenate([near_keys_all] + [p[rs] for p in far_pieces], axis=0)
        far_cols = jnp.broadcast_to(seen[:, blk][None, :, None], (BLK, len(offsets), BLK))
        visible = jnp.concatenate(
            [near_mask[rs], far_cols.reshape(BLK, len(offsets) * BLK)], axis=1
        )
        out_b, dq_b, weights, dscores, log_total, row_delta = attend_parts(
            query_tokens[rs], grad_out[rs], kv, visible
        )
        terms_b = key_terms(weights, dscores, query_tokens[rs], grad_out[rs])
        outs.append(out_b)
        dqs.append(dq_b)
        near_parts.append(terms_b[: 3 * tok_rows])
        far_parts.append(terms_b[3 * tok_rows :])
    attention_out = jnp.concatenate(outs, axis=0)
    query_grad = jnp.concatenate(dqs, axis=0)
    near_terms = sum(near_parts[1:], near_parts[0])
    far_terms = jnp.concatenate(
        [
            jnp.concatenate([part[i * BLK : (i + 1) * BLK] for part in far_parts], axis=0)
            for i in range(len(offsets))
        ],
        axis=0,
    )
    sent = near_terms.astype(jnp.bfloat16)
    from_after = from_behind(sent[:tok_rows], "seq", -1).astype(jnp.float32)
    from_before = from_behind(sent[2 * tok_rows :], "seq", 1).astype(jnp.float32)
    grad_total = near_terms[tok_rows : 2 * tok_rows] + from_after + from_before
    for slot_index in range(len(offsets)):
        first_row = slot_index * 2 * BLK
        grad_piece = far_terms[first_row : first_row + 2 * BLK].astype(jnp.bfloat16)
        if offsets[slot_index] == half:
            returned = lax.ppermute(
                grad_piece, "seq", [(src, (src + half) % frame_count) for src in range(frame_count)]
            )
        else:
            returned = from_behind(grad_piece, "seq", offsets[slot_index])
        returned = returned.astype(jnp.float32)
        current = grad_total
        grad_total = current + returned
    key_grad = grad_total[:, :HD]
    value_grad = grad_total[:, HD:]
    return (attention_out, query_grad, key_grad, value_grad)


def solution(mesh):
    return jax.shard_map(
        shards,
        mesh=mesh,
        in_specs=(P("seq", "head"), P("seq", "head"), P("seq", "head"), P("seq", "head"), P()),
        out_specs=(P("seq", "head"), P("seq", "head"), P("seq", "head"), P("seq", "head")),
        check_vma=False,
    )
```

```python
import jax
import jax.numpy as jnp
from jax import lax
from jax.sharding import PartitionSpec as P

HD = 128
BLK = 128


def extended(shard, sides, width):
    for axis, dim in sides:
        size, length = (lax.axis_size(axis), shard.shape[dim])
        up = [(i, (i + 1) % size) for i in range(size - 1)]
        down = [(j, i) for i, j in up]
        last = lax.slice_in_dim(shard, length - width, length, axis=dim)
        leading = lax.slice_in_dim(shard, 0, width, axis=dim)
        before = lax.ppermute(last, axis, up)
        after = lax.ppermute(leading, axis, down)
        shard = jnp.concatenate([before, shard, after], axis=dim)
    return shard


def from_behind(value, axis, steps):
    count = lax.axis_size(axis)
    leading, last = (max(0, -steps), min(count, count - steps))
    return lax.ppermute(value, axis, [(source, source + steps) for source in range(leading, last)])


def offsets_for(frame_count):
    distances = [2, 3]
    power_step = 4
    while power_step < frame_count:
        distances.append(power_step)
        power_step = power_step * 2
    return [sign_value * distance_step for distance_step in distances for sign_value in (1, -1)]


def far_window(entries, is_valid):
    pair_start = jnp.maximum(entries[0], 0)
    pair_index = jnp.arange(2, dtype=jnp.int32)
    far_hit = (
        is_valid & (entries[:, None] >= 0) & (entries[:, None] - pair_start == pair_index[None, :])
    )
    far_hit = jnp.repeat(jnp.repeat(far_hit, BLK, axis=0), BLK, axis=1)
    return (pair_start, far_hit)


def attend_parts(queries, grads_out, keys_all, visible):
    score_scale = HD ** (-0.5)
    across = (((1,), (1,)), ((), ()))
    key_part = keys_all[:, :HD]
    value_part = keys_all[:, HD:]
    scores = (
        lax.dot_general(queries, key_part, across, preferred_element_type=jnp.float32) * score_scale
    )
    scores = jnp.where(visible, scores, -jnp.inf)
    row_max = jnp.max(scores, axis=1, keepdims=True)
    row_total = jnp.sum(jnp.exp(scores - row_max), axis=1, keepdims=True)
    log_total = row_max + jnp.log(row_total)
    weights = jnp.exp(scores - log_total).astype(jnp.bfloat16)
    out_rows = jnp.dot(weights, value_part, preferred_element_type=jnp.float32)
    row_delta = jnp.sum(out_rows * grads_out.astype(jnp.float32), axis=1, keepdims=True)
    dweights = lax.dot_general(grads_out, value_part, across, preferred_element_type=jnp.float32)
    dscores = (weights.astype(jnp.float32) * (dweights - row_delta)).astype(jnp.bfloat16)
    query_rows_grad = jnp.dot(dscores, key_part, preferred_element_type=jnp.float32) * score_scale
    return (out_rows, query_rows_grad, weights, dscores, log_total, row_delta)


def key_terms(weights, dscores, queries, grads_out):
    score_scale = HD ** (-0.5)
    over_rows = (((0,), (0,)), ((), ()))
    key_side = (
        lax.dot_general(dscores, queries, over_rows, preferred_element_type=jnp.float32)
        * score_scale
    )
    value_side = lax.dot_general(weights, grads_out, over_rows, preferred_element_type=jnp.float32)
    return jnp.concatenate([key_side, value_side], axis=1)


def shards(query_tokens, key_tokens, value_tokens, grad_out, far_block):
    tok_rows = query_tokens.shape[0]
    frame_count = lax.axis_size("seq")
    device = lax.axis_index("seq")
    offsets = offsets_for(frame_count)
    joined = jnp.concatenate([key_tokens, value_tokens], axis=1)
    near_keys = extended(joined, (("seq", 0),), tok_rows)
    neighbour = device + jnp.arange(3, dtype=jnp.int32) - 1
    near_ok = (neighbour >= 0) & (neighbour < frame_count)
    pieces = [near_keys]
    half = frame_count // 2
    offsets = [o for o in (8, -8, half, 4, -4, 32, -32, 3, -3, 16, -16, 2, -2) if o in offsets]
    for offset in offsets:
        if offset == half:
            arrived = lax.ppermute(
                joined, "seq", [(src, (src + half) % frame_count) for src in range(frame_count)]
            )
        else:
            arrived = from_behind(joined, "seq", -offset)
        pieces.append(arrived)
    shifts = jnp.asarray(offsets, jnp.int32)
    other_frame = jnp.where(shifts == half, (device + half) % frame_count, device + shifts)
    is_valid = (other_frame >= 0) & (other_frame < frame_count)
    frame_rows = lax.dynamic_index_in_dim(far_block, device, 0, keepdims=False)
    entries = jnp.take(frame_rows, jnp.clip(other_frame, 0, frame_count - 1), axis=0)
    seen = is_valid[:, None] & (entries >= 0)
    blocks = tok_rows // BLK
    row_block = jnp.arange(tok_rows, dtype=jnp.int32) // BLK
    near_mask = jnp.broadcast_to(
        near_ok[None, :, None], (tok_rows, 3, tok_rows)
    ).reshape(tok_rows, 3 * tok_rows)
    seen_rows = jnp.take(seen, row_block, axis=1)
    diag = row_block[:, None] == row_block[None, :]
    far_mask = (diag[:, None, :] & seen_rows.T[:, :, None]).reshape(
        tok_rows, len(offsets) * tok_rows
    )
    keys_all = jnp.concatenate(pieces, axis=0)
    visible = jnp.concatenate([near_mask, far_mask], axis=1)
    attention_out, query_grad, weights, dscores, log_total, row_delta = attend_parts(
        query_tokens, grad_out, keys_all, visible
    )
    near_terms = key_terms(
        weights[:, : 3 * tok_rows], dscores[:, : 3 * tok_rows], query_tokens, grad_out
    )
    sent = near_terms.astype(jnp.bfloat16)
    from_after = from_behind(sent[:tok_rows], "seq", -1).astype(jnp.float32)
    from_before = from_behind(sent[2 * tok_rows :], "seq", 1).astype(jnp.float32)
    grad_total = near_terms[tok_rows : 2 * tok_rows] + from_after + from_before
    far_terms = key_terms(
        weights[:, 3 * tok_rows :], dscores[:, 3 * tok_rows :], query_tokens, grad_out
    )
    for slot_index in range(len(offsets)):
        first_row = slot_index * 2 * BLK
        grad_piece = far_terms[first_row : first_row + 2 * BLK].astype(jnp.bfloat16)
        if offsets[slot_index] == half:
            returned = lax.ppermute(
                grad_piece, "seq", [(src, (src + half) % frame_count) for src in range(frame_count)]
            )
        else:
            returned = from_behind(grad_piece, "seq", offsets[slot_index])
        returned = returned.astype(jnp.float32)
        current = grad_total
        grad_total = current + returned
    key_grad = grad_total[:, :HD]
    value_grad = grad_total[:, HD:]
    return (attention_out, query_grad, key_grad, value_grad)


def solution(mesh):
    return jax.shard_map(
        shards,
        mesh=mesh,
        in_specs=(P("seq", "head"), P("seq", "head"), P("seq", "head"), P("seq", "head"), P()),
        out_specs=(P("seq", "head"), P("seq", "head"), P("seq", "head"), P("seq", "head")),
        check_vma=False,
    )
```

```python
import jax
import jax.numpy as jnp
from jax import lax
from jax.sharding import PartitionSpec as P

HD = 128
BLK = 128


def extended(shard, sides, width):
    for axis, dim in sides:
        size, length = (lax.axis_size(axis), shard.shape[dim])
        up = [(i, (i + 1) % size) for i in range(size - 1)]
        down = [(j, i) for i, j in up]
        last = lax.slice_in_dim(shard, length - width, length, axis=dim)
        leading = lax.slice_in_dim(shard, 0, width, axis=dim)
        before = lax.ppermute(last, axis, up)
        after = lax.ppermute(leading, axis, down)
        shard = jnp.concatenate([before, shard, after], axis=dim)
    return shard


def from_behind(value, axis, steps):
    count = lax.axis_size(axis)
    leading, last = (max(0, -steps), min(count, count - steps))
    return lax.ppermute(value, axis, [(source, source + steps) for source in range(leading, last)])


def offsets_for(frame_count):
    distances = [2, 3]
    power_step = 4
    while power_step < frame_count:
        distances.append(power_step)
        power_step = power_step * 2
    return [sign_value * distance_step for distance_step in distances for sign_value in (1, -1)]


def far_window(entries, is_valid):
    pair_start = jnp.maximum(entries[0], 0)
    pair_index = jnp.arange(2, dtype=jnp.int32)
    far_hit = (
        is_valid & (entries[:, None] >= 0) & (entries[:, None] - pair_start == pair_index[None, :])
    )
    far_hit = jnp.repeat(jnp.repeat(far_hit, BLK, axis=0), BLK, axis=1)
    return (pair_start, far_hit)


def attend_parts(queries, grads_out, keys_all, visible):
    score_scale = HD ** (-0.5)
    across = (((1,), (1,)), ((), ()))
    key_part = keys_all[:, :HD]
    value_part = keys_all[:, HD:]
    scores = (
        lax.dot_general(queries, key_part, across, preferred_element_type=jnp.float32) * score_scale
    )
    scores = jnp.where(visible, scores, -jnp.inf)
    row_max = jnp.max(scores, axis=1, keepdims=True)
    row_total = jnp.sum(jnp.exp(scores - row_max), axis=1, keepdims=True)
    log_total = row_max + jnp.log(row_total)
    weights = jnp.exp(scores - log_total).astype(jnp.bfloat16)
    out_rows = jnp.dot(weights, value_part, preferred_element_type=jnp.float32)
    row_delta = jnp.sum(out_rows * grads_out.astype(jnp.float32), axis=1, keepdims=True)
    dweights = lax.dot_general(grads_out, value_part, across, preferred_element_type=jnp.float32)
    dscores = (weights.astype(jnp.float32) * (dweights - row_delta)).astype(jnp.bfloat16)
    query_rows_grad = jnp.dot(dscores, key_part, preferred_element_type=jnp.float32) * score_scale
    return (out_rows, query_rows_grad, weights, dscores, log_total, row_delta)


def key_terms(weights, dscores, queries, grads_out):
    score_scale = HD ** (-0.5)
    over_rows = (((0,), (0,)), ((), ()))
    key_side = (
        lax.dot_general(dscores, queries, over_rows, preferred_element_type=jnp.float32)
        * score_scale
    )
    value_side = lax.dot_general(weights, grads_out, over_rows, preferred_element_type=jnp.float32)
    return jnp.concatenate([key_side, value_side], axis=1)


def shards(query_tokens, key_tokens, value_tokens, grad_out, far_block):
    tok_rows = query_tokens.shape[0]
    frame_count = lax.axis_size("seq")
    device = lax.axis_index("seq")
    offsets = offsets_for(frame_count)
    joined = jnp.concatenate([key_tokens, value_tokens], axis=1)
    near_keys = extended(joined, (("seq", 0),), tok_rows)
    neighbour = device + jnp.arange(3, dtype=jnp.int32) - 1
    near_ok = (neighbour >= 0) & (neighbour < frame_count)
    pieces = [near_keys]
    half = frame_count // 2
    offsets = [o for o in (8, half, -8, 32, 4, -32, -4, 16, 3, -16, -3, 2, -2) if o in offsets]
    for offset in offsets:
        if offset == half:
            arrived = lax.ppermute(
                joined, "seq", [(src, (src + half) % frame_count) for src in range(frame_count)]
            )
        else:
            arrived = from_behind(joined, "seq", -offset)
        pieces.append(arrived)
    shifts = jnp.asarray(offsets, jnp.int32)
    other_frame = jnp.where(shifts == half, (device + half) % frame_count, device + shifts)
    is_valid = (other_frame >= 0) & (other_frame < frame_count)
    frame_rows = lax.dynamic_index_in_dim(far_block, device, 0, keepdims=False)
    entries = jnp.take(frame_rows, jnp.clip(other_frame, 0, frame_count - 1), axis=0)
    seen = is_valid[:, None] & (entries >= 0)
    blocks = tok_rows // BLK
    row_block = jnp.arange(tok_rows, dtype=jnp.int32) // BLK
    near_mask = jnp.broadcast_to(
        near_ok[None, :, None], (tok_rows, 3, tok_rows)
    ).reshape(tok_rows, 3 * tok_rows)
    seen_rows = jnp.take(seen, row_block, axis=1)
    diag = row_block[:, None] == row_block[None, :]
    far_mask = (diag[:, None, :] & seen_rows.T[:, :, None]).reshape(
        tok_rows, len(offsets) * tok_rows
    )
    keys_all = jnp.concatenate(pieces, axis=0)
    visible = jnp.concatenate([near_mask, far_mask], axis=1)
    attention_out, query_grad, weights, dscores, log_total, row_delta = attend_parts(
        query_tokens, grad_out, keys_all, visible
    )
    near_terms = key_terms(
        weights[:, : 3 * tok_rows], dscores[:, : 3 * tok_rows], query_tokens, grad_out
    )
    sent = near_terms.astype(jnp.bfloat16)
    from_after = from_behind(sent[:tok_rows], "seq", -1).astype(jnp.float32)
    from_before = from_behind(sent[2 * tok_rows :], "seq", 1).astype(jnp.float32)
    grad_total = near_terms[tok_rows : 2 * tok_rows] + from_after + from_before
    far_terms = key_terms(
        weights[:, 3 * tok_rows :], dscores[:, 3 * tok_rows :], query_tokens, grad_out
    )
    for slot_index in range(len(offsets)):
        first_row = slot_index * 2 * BLK
        grad_piece = far_terms[first_row : first_row + 2 * BLK].astype(jnp.bfloat16)
        if offsets[slot_index] == half:
            returned = lax.ppermute(
                grad_piece, "seq", [(src, (src + half) % frame_count) for src in range(frame_count)]
            )
        else:
            returned = from_behind(grad_piece, "seq", offsets[slot_index])
        returned = returned.astype(jnp.float32)
        current = grad_total
        grad_total = current + returned
    key_grad = grad_total[:, :HD]
    value_grad = grad_total[:, HD:]
    return (attention_out, query_grad, key_grad, value_grad)


def solution(mesh):
    return jax.shard_map(
        shards,
        mesh=mesh,
        in_specs=(P("seq", "head"), P("seq", "head"), P("seq", "head"), P("seq", "head"), P()),
        out_specs=(P("seq", "head"), P("seq", "head"), P("seq", "head"), P("seq", "head")),
        check_vma=False,
    )
```

```python
import jax
import jax.numpy as jnp
from jax import lax
from jax.sharding import PartitionSpec as P

HD = 128
BLK = 128


def extended(shard, sides, width):
    for axis, dim in sides:
        size, length = (lax.axis_size(axis), shard.shape[dim])
        up = [(i, (i + 1) % size) for i in range(size - 1)]
        down = [(j, i) for i, j in up]
        last = lax.slice_in_dim(shard, length - width, length, axis=dim)
        leading = lax.slice_in_dim(shard, 0, width, axis=dim)
        before = lax.ppermute(last, axis, up)
        after = lax.ppermute(leading, axis, down)
        shard = jnp.concatenate([before, shard, after], axis=dim)
    return shard


def from_behind(value, axis, steps):
    count = lax.axis_size(axis)
    leading, last = (max(0, -steps), min(count, count - steps))
    return lax.ppermute(value, axis, [(source, source + steps) for source in range(leading, last)])


def offsets_for(frame_count):
    distances = [2, 3]
    power_step = 4
    while power_step < frame_count:
        distances.append(power_step)
        power_step = power_step * 2
    return [sign_value * distance_step for distance_step in distances for sign_value in (1, -1)]


def far_window(entries, is_valid):
    pair_start = jnp.maximum(entries[0], 0)
    pair_index = jnp.arange(2, dtype=jnp.int32)
    far_hit = (
        is_valid & (entries[:, None] >= 0) & (entries[:, None] - pair_start == pair_index[None, :])
    )
    far_hit = jnp.repeat(jnp.repeat(far_hit, BLK, axis=0), BLK, axis=1)
    return (pair_start, far_hit)


def attend_parts(queries, grads_out, keys_all, visible):
    score_scale = HD ** (-0.5)
    across = (((1,), (1,)), ((), ()))
    key_part = keys_all[:, :HD]
    value_part = keys_all[:, HD:]
    scores = (
        lax.dot_general(queries, key_part, across, preferred_element_type=jnp.float32) * score_scale
    )
    scores = jnp.where(visible, scores, -jnp.inf)
    row_max = jnp.max(scores, axis=1, keepdims=True)
    row_total = jnp.sum(jnp.exp(scores - row_max), axis=1, keepdims=True)
    log_total = row_max + jnp.log(row_total)
    weights = jnp.exp(scores - log_total).astype(jnp.bfloat16)
    out_rows = jnp.dot(weights, value_part, preferred_element_type=jnp.float32)
    row_delta = jnp.sum(out_rows * grads_out.astype(jnp.float32), axis=1, keepdims=True)
    dweights = lax.dot_general(grads_out, value_part, across, preferred_element_type=jnp.float32)
    dscores = (weights.astype(jnp.float32) * (dweights - row_delta)).astype(jnp.bfloat16)
    query_rows_grad = jnp.dot(dscores, key_part, preferred_element_type=jnp.float32) * score_scale
    return (out_rows, query_rows_grad, weights, dscores, log_total, row_delta)


def key_terms(weights, dscores, queries, grads_out):
    score_scale = HD ** (-0.5)
    over_rows = (((0,), (0,)), ((), ()))
    key_side = (
        lax.dot_general(dscores, queries, over_rows, preferred_element_type=jnp.float32)
        * score_scale
    )
    value_side = lax.dot_general(weights, grads_out, over_rows, preferred_element_type=jnp.float32)
    return jnp.concatenate([key_side, value_side], axis=1)


def shards(query_tokens, key_tokens, value_tokens, grad_out, far_block):
    tok_rows = query_tokens.shape[0]
    frame_count = lax.axis_size("seq")
    device = lax.axis_index("seq")
    offsets = offsets_for(frame_count)
    joined = jnp.concatenate([key_tokens, value_tokens], axis=1)
    near_keys = extended(joined, (("seq", 0),), tok_rows)
    neighbour = device + jnp.arange(3, dtype=jnp.int32) - 1
    near_ok = (neighbour >= 0) & (neighbour < frame_count)
    pieces = [near_keys]
    half = frame_count // 2
    offsets = [o for o in (8, -8, half, 4, -4, 32, -32, 3, -3, 16, -16, 2, -2) if o in offsets]
    for offset in offsets:
        if offset == half:
            arrived = lax.ppermute(
                joined, "seq", [(src, (src + half) % frame_count) for src in range(frame_count)]
            )
        else:
            arrived = from_behind(joined, "seq", -offset)
        pieces.append(arrived)
    shifts = jnp.asarray(offsets, jnp.int32)
    other_frame = jnp.where(shifts == half, (device + half) % frame_count, device + shifts)
    is_valid = (other_frame >= 0) & (other_frame < frame_count)
    frame_rows = lax.dynamic_index_in_dim(far_block, device, 0, keepdims=False)
    entries = jnp.take(frame_rows, jnp.clip(other_frame, 0, frame_count - 1), axis=0)
    seen = is_valid[:, None] & (entries >= 0)
    blocks = tok_rows // BLK
    row_block = jnp.arange(tok_rows, dtype=jnp.int32) // BLK
    near_mask = jnp.broadcast_to(
        near_ok[None, :, None], (tok_rows, 3, tok_rows)
    ).reshape(tok_rows, 3 * tok_rows)
    seen_rows = jnp.take(seen, row_block, axis=1)
    diag = row_block[:, None] == row_block[None, :]
    far_mask = (diag[:, None, :] & seen_rows.T[:, :, None]).reshape(
        tok_rows, len(offsets) * tok_rows
    )
    keys_all = jnp.concatenate(pieces, axis=0)
    visible = jnp.concatenate([near_mask, far_mask], axis=1)
    attention_out, query_grad, weights, dscores, log_total, row_delta = attend_parts(
        query_tokens, grad_out, keys_all, visible
    )
    near_terms = key_terms(
        weights[:, : 3 * tok_rows], dscores[:, : 3 * tok_rows], query_tokens, grad_out
    )
    sent = near_terms.astype(jnp.bfloat16)
    from_after = from_behind(sent[:tok_rows], "seq", -1).astype(jnp.float32)
    from_before = from_behind(sent[2 * tok_rows :], "seq", 1).astype(jnp.float32)
    grad_total = near_terms[tok_rows : 2 * tok_rows] + from_after + from_before
    far_terms = key_terms(
        weights[:, 3 * tok_rows :], dscores[:, 3 * tok_rows :], query_tokens, grad_out
    )
    for slot_index in reversed(range(len(offsets))):
        first_row = slot_index * 2 * BLK
        grad_piece = far_terms[first_row : first_row + 2 * BLK].astype(jnp.bfloat16)
        if offsets[slot_index] == half:
            returned = lax.ppermute(
                grad_piece, "seq", [(src, (src + half) % frame_count) for src in range(frame_count)]
            )
        else:
            returned = from_behind(grad_piece, "seq", offsets[slot_index])
        returned = returned.astype(jnp.float32)
        current = grad_total
        grad_total = current + returned
    key_grad = grad_total[:, :HD]
    value_grad = grad_total[:, HD:]
    return (attention_out, query_grad, key_grad, value_grad)


def solution(mesh):
    return jax.shard_map(
        shards,
        mesh=mesh,
        in_specs=(P("seq", "head"), P("seq", "head"), P("seq", "head"), P("seq", "head"), P()),
        out_specs=(P("seq", "head"), P("seq", "head"), P("seq", "head"), P("seq", "head")),
        check_vma=False,
    )
```

```python
import jax
import jax.numpy as jnp
from jax import lax
from jax.sharding import PartitionSpec as P

HD = 128
BLK = 128


def extended(shard, sides, width):
    for axis, dim in sides:
        size, length = (lax.axis_size(axis), shard.shape[dim])
        up = [(i, (i + 1) % size) for i in range(size - 1)]
        down = [(j, i) for i, j in up]
        last = lax.slice_in_dim(shard, length - width, length, axis=dim)
        leading = lax.slice_in_dim(shard, 0, width, axis=dim)
        before = lax.ppermute(last, axis, up)
        after = lax.ppermute(leading, axis, down)
        shard = jnp.concatenate([before, shard, after], axis=dim)
    return shard


def from_behind(value, axis, steps):
    count = lax.axis_size(axis)
    leading, last = (max(0, -steps), min(count, count - steps))
    return lax.ppermute(value, axis, [(source, source + steps) for source in range(leading, last)])


def offsets_for(frame_count):
    distances = [2, 3]
    power_step = 4
    while power_step < frame_count:
        distances.append(power_step)
        power_step = power_step * 2
    return [sign_value * distance_step for distance_step in distances for sign_value in (1, -1)]


def far_window(entries, is_valid):
    pair_start = jnp.maximum(entries[0], 0)
    pair_index = jnp.arange(2, dtype=jnp.int32)
    far_hit = (
        is_valid & (entries[:, None] >= 0) & (entries[:, None] - pair_start == pair_index[None, :])
    )
    far_hit = jnp.repeat(jnp.repeat(far_hit, BLK, axis=0), BLK, axis=1)
    return (pair_start, far_hit)


def attend_parts(queries, grads_out, keys_all, visible):
    score_scale = HD ** (-0.5)
    across = (((1,), (1,)), ((), ()))
    key_part = keys_all[:, :HD]
    value_part = keys_all[:, HD:]
    scores = (
        lax.dot_general(queries, key_part, across, preferred_element_type=jnp.float32) * score_scale
    )
    scores = jnp.where(visible, scores, -jnp.inf)
    row_max = jnp.max(scores, axis=1, keepdims=True)
    row_total = jnp.sum(jnp.exp(scores - row_max), axis=1, keepdims=True)
    log_total = row_max + jnp.log(row_total)
    weights = jnp.exp(scores - log_total).astype(jnp.bfloat16)
    out_rows = jnp.dot(weights, value_part, preferred_element_type=jnp.float32)
    row_delta = jnp.sum(out_rows * grads_out.astype(jnp.float32), axis=1, keepdims=True)
    dweights = lax.dot_general(grads_out, value_part, across, preferred_element_type=jnp.float32)
    dscores = (weights.astype(jnp.float32) * (dweights - row_delta)).astype(jnp.bfloat16)
    query_rows_grad = jnp.dot(dscores, key_part, preferred_element_type=jnp.float32) * score_scale
    return (out_rows, query_rows_grad, weights, dscores, log_total, row_delta)


def key_terms(weights, dscores, queries, grads_out):
    score_scale = HD ** (-0.5)
    over_rows = (((0,), (0,)), ((), ()))
    key_side = (
        lax.dot_general(dscores, queries, over_rows, preferred_element_type=jnp.float32)
        * score_scale
    )
    value_side = lax.dot_general(weights, grads_out, over_rows, preferred_element_type=jnp.float32)
    return jnp.concatenate([key_side, value_side], axis=1)


def shards(query_tokens, key_tokens, value_tokens, grad_out, far_block):
    tok_rows = query_tokens.shape[0]
    frame_count = lax.axis_size("seq")
    device = lax.axis_index("seq")
    offsets = offsets_for(frame_count)
    joined = jnp.concatenate([key_tokens, value_tokens], axis=1)
    near_keys = extended(joined, (("seq", 0),), tok_rows)
    neighbour = device + jnp.arange(3, dtype=jnp.int32) - 1
    near_ok = (neighbour >= 0) & (neighbour < frame_count)
    pieces = [near_keys]
    half = frame_count // 2
    offsets = [o for o in (half, 8, -8, 32, -32, 4, -4, 16, -16, 3, -3, 2, -2) if o in offsets]
    for offset in offsets:
        if offset == half:
            arrived = lax.ppermute(
                joined, "seq", [(src, (src + half) % frame_count) for src in range(frame_count)]
            )
        else:
            arrived = from_behind(joined, "seq", -offset)
        pieces.append(arrived)
    shifts = jnp.asarray(offsets, jnp.int32)
    other_frame = jnp.where(shifts == half, (device + half) % frame_count, device + shifts)
    is_valid = (other_frame >= 0) & (other_frame < frame_count)
    frame_rows = lax.dynamic_index_in_dim(far_block, device, 0, keepdims=False)
    entries = jnp.take(frame_rows, jnp.clip(other_frame, 0, frame_count - 1), axis=0)
    seen = is_valid[:, None] & (entries >= 0)
    blocks = tok_rows // BLK
    row_block = jnp.arange(tok_rows, dtype=jnp.int32) // BLK
    near_mask = jnp.broadcast_to(
        near_ok[None, :, None], (tok_rows, 3, tok_rows)
    ).reshape(tok_rows, 3 * tok_rows)
    seen_rows = jnp.take(seen, row_block, axis=1)
    diag = row_block[:, None] == row_block[None, :]
    far_mask = (diag[:, None, :] & seen_rows.T[:, :, None]).reshape(
        tok_rows, len(offsets) * tok_rows
    )
    keys_all = jnp.concatenate(pieces, axis=0)
    visible = jnp.concatenate([near_mask, far_mask], axis=1)
    attention_out, query_grad, weights, dscores, log_total, row_delta = attend_parts(
        query_tokens, grad_out, keys_all, visible
    )
    near_terms = key_terms(
        weights[:, : 3 * tok_rows], dscores[:, : 3 * tok_rows], query_tokens, grad_out
    )
    sent = near_terms.astype(jnp.bfloat16)
    from_after = from_behind(sent[:tok_rows], "seq", -1).astype(jnp.float32)
    from_before = from_behind(sent[2 * tok_rows :], "seq", 1).astype(jnp.float32)
    grad_total = near_terms[tok_rows : 2 * tok_rows] + from_after + from_before
    far_terms = key_terms(
        weights[:, 3 * tok_rows :], dscores[:, 3 * tok_rows :], query_tokens, grad_out
    )
    for slot_index in range(len(offsets)):
        first_row = slot_index * 2 * BLK
        grad_piece = far_terms[first_row : first_row + 2 * BLK].astype(jnp.bfloat16)
        if offsets[slot_index] == half:
            returned = lax.ppermute(
                grad_piece, "seq", [(src, (src + half) % frame_count) for src in range(frame_count)]
            )
        else:
            returned = from_behind(grad_piece, "seq", offsets[slot_index])
        returned = returned.astype(jnp.float32)
        current = grad_total
        grad_total = current + returned
    key_grad = grad_total[:, :HD]
    value_grad = grad_total[:, HD:]
    return (attention_out, query_grad, key_grad, value_grad)


def solution(mesh):
    return jax.shard_map(
        shards,
        mesh=mesh,
        in_specs=(P("seq", "head"), P("seq", "head"), P("seq", "head"), P("seq", "head"), P()),
        out_specs=(P("seq", "head"), P("seq", "head"), P("seq", "head"), P("seq", "head")),
        check_vma=False,
    )
```

```python
import jax
import jax.numpy as jnp
from jax import lax
from jax.sharding import PartitionSpec as P

HD = 128
BLK = 128


def extended(shard, sides, width):
    for axis, dim in sides:
        size, length = (lax.axis_size(axis), shard.shape[dim])
        up = [(i, (i + 1) % size) for i in range(size - 1)]
        down = [(j, i) for i, j in up]
        last = lax.slice_in_dim(shard, length - width, length, axis=dim)
        leading = lax.slice_in_dim(shard, 0, width, axis=dim)
        before = lax.ppermute(last, axis, up)
        after = lax.ppermute(leading, axis, down)
        shard = jnp.concatenate([before, shard, after], axis=dim)
    return shard


def from_behind(value, axis, steps):
    count = lax.axis_size(axis)
    leading, last = (max(0, -steps), min(count, count - steps))
    return lax.ppermute(value, axis, [(source, source + steps) for source in range(leading, last)])


def offsets_for(frame_count):
    distances = [2, 3]
    power_step = 4
    while power_step < frame_count:
        distances.append(power_step)
        power_step = power_step * 2
    return [sign_value * distance_step for distance_step in distances for sign_value in (1, -1)]


def far_window(entries, is_valid):
    pair_start = jnp.maximum(entries[0], 0)
    pair_index = jnp.arange(2, dtype=jnp.int32)
    far_hit = (
        is_valid & (entries[:, None] >= 0) & (entries[:, None] - pair_start == pair_index[None, :])
    )
    far_hit = jnp.repeat(jnp.repeat(far_hit, BLK, axis=0), BLK, axis=1)
    return (pair_start, far_hit)


def attend_parts(queries, grads_out, keys_all, visible):
    score_scale = HD ** (-0.5)
    across = (((1,), (1,)), ((), ()))
    key_part = keys_all[:, :HD]
    value_part = keys_all[:, HD:]
    scores = (
        lax.dot_general(queries, key_part, across, preferred_element_type=jnp.float32) * score_scale
    )
    scores = jnp.where(visible, scores, -jnp.inf)
    row_max = jnp.max(scores, axis=1, keepdims=True)
    row_total = jnp.sum(jnp.exp(scores - row_max), axis=1, keepdims=True)
    log_total = row_max + jnp.log(row_total)
    weights = jnp.exp(scores - log_total).astype(jnp.bfloat16)
    out_rows = jnp.dot(weights, value_part, preferred_element_type=jnp.float32)
    row_delta = jnp.sum(out_rows * grads_out.astype(jnp.float32), axis=1, keepdims=True)
    dweights = lax.dot_general(grads_out, value_part, across, preferred_element_type=jnp.float32)
    dscores = (weights.astype(jnp.float32) * (dweights - row_delta)).astype(jnp.bfloat16)
    query_rows_grad = jnp.dot(dscores, key_part, preferred_element_type=jnp.float32) * score_scale
    return (out_rows, query_rows_grad, weights, dscores, log_total, row_delta)


def key_terms(weights, dscores, queries, grads_out):
    score_scale = HD ** (-0.5)
    over_rows = (((0,), (0,)), ((), ()))
    key_side = (
        lax.dot_general(dscores, queries, over_rows, preferred_element_type=jnp.float32)
        * score_scale
    )
    value_side = lax.dot_general(weights, grads_out, over_rows, preferred_element_type=jnp.float32)
    return jnp.concatenate([key_side, value_side], axis=1)


def shards(query_tokens, key_tokens, value_tokens, grad_out, far_block):
    tok_rows = query_tokens.shape[0]
    frame_count = lax.axis_size("seq")
    device = lax.axis_index("seq")
    offsets = offsets_for(frame_count)
    joined = jnp.concatenate([key_tokens, value_tokens], axis=1)
    near_keys = extended(joined, (("seq", 0),), tok_rows)
    neighbour = device + jnp.arange(3, dtype=jnp.int32) - 1
    near_ok = (neighbour >= 0) & (neighbour < frame_count)
    pieces = [near_keys]
    half = frame_count // 2
    offsets = [o for o in (8, -8, half, 4, -4, 32, -32, 3, -3, 16, -16, 2, -2) if o in offsets]
    for offset in offsets:
        if offset == half:
            arrived = lax.ppermute(
                joined, "seq", [(src, (src + half) % frame_count) for src in range(frame_count)]
            )
        else:
            arrived = from_behind(joined, "seq", -offset)
        pieces.append(arrived)
    shifts = jnp.asarray(offsets, jnp.int32)
    other_frame = jnp.where(shifts == half, (device + half) % frame_count, device + shifts)
    is_valid = (other_frame >= 0) & (other_frame < frame_count)
    frame_rows = lax.dynamic_index_in_dim(far_block, device, 0, keepdims=False)
    entries = jnp.take(frame_rows, jnp.clip(other_frame, 0, frame_count - 1), axis=0)
    seen = is_valid[:, None] & (entries >= 0)
    blocks = tok_rows // BLK
    row_block = jnp.arange(tok_rows, dtype=jnp.int32) // BLK
    near_mask = jnp.broadcast_to(
        near_ok[None, :, None], (tok_rows, 3, tok_rows)
    ).reshape(tok_rows, 3 * tok_rows)
    seen_rows = jnp.take(seen, row_block, axis=1)
    diag = row_block[:, None] == row_block[None, :]
    far_mask = (diag[:, None, :] & seen_rows.T[:, :, None]).reshape(
        tok_rows, len(offsets) * tok_rows
    )
    keys_all = jnp.concatenate(pieces, axis=0)
    visible = jnp.concatenate([near_mask, far_mask], axis=1)
    attention_out, query_grad, weights, dscores, log_total, row_delta = attend_parts(
        query_tokens, grad_out, keys_all, visible
    )
    near_terms = key_terms(
        weights[:, : 3 * tok_rows], dscores[:, : 3 * tok_rows], query_tokens, grad_out
    )
    grad_total = near_terms[tok_rows : 2 * tok_rows]
    far_terms = key_terms(
        weights[:, 3 * tok_rows :], dscores[:, 3 * tok_rows :], query_tokens, grad_out
    )
    for slot_index in range(len(offsets)):
        first_row = slot_index * 2 * BLK
        grad_piece = far_terms[first_row : first_row + 2 * BLK].astype(jnp.bfloat16)
        if offsets[slot_index] == half:
            returned = lax.ppermute(
                grad_piece, "seq", [(src, (src + half) % frame_count) for src in range(frame_count)]
            )
        else:
            returned = from_behind(grad_piece, "seq", offsets[slot_index])
        returned = returned.astype(jnp.float32)
        current = grad_total
        grad_total = current + returned
    sent = near_terms.astype(jnp.bfloat16)
    from_after = from_behind(sent[:tok_rows], "seq", -1).astype(jnp.float32)
    from_before = from_behind(sent[2 * tok_rows :], "seq", 1).astype(jnp.float32)
    grad_total = grad_total + from_after + from_before
    key_grad = grad_total[:, :HD]
    value_grad = grad_total[:, HD:]
    return (attention_out, query_grad, key_grad, value_grad)


def solution(mesh):
    return jax.shard_map(
        shards,
        mesh=mesh,
        in_specs=(P("seq", "head"), P("seq", "head"), P("seq", "head"), P("seq", "head"), P()),
        out_specs=(P("seq", "head"), P("seq", "head"), P("seq", "head"), P("seq", "head")),
        check_vma=False,
    )
```
